512 devices in a mesh: tri: 32 (over y, z_lo), vir: 16 (over x, z_hi, core).
Axes of the slice: x: 4, y: 8, z: 8 (z_hi: 2, z_lo: 4; z = z_hi * 4 + z_lo), core: 2. Of those that a mesh axis runs over, the one named last changes fastest.
Arguments:
- amps: bfloat16 [96, 768, 768], P('tri', 'vir'), may hold values from -0.21875 to 0.21875
- vvvo: bfloat16 [96, 768, 128], P('tri', 'vir'), may hold values from -6 to 6
- occ_gap: float32 [64], replicated, may hold values from 0.3 to 1
- vir_gap: float32 [768], P('vir'), may hold values from 0.5 to 2
- pair_gap: float32 [128], replicated, may hold values from 0.5 to 2
- block_sizes: int32 [32], replicated, may hold values from 1 to 3, 64 in all
- roots: int32 [32], replicated, may hold values from 0 to 31, each once
- triples: int32 [384, 2], P('tri'), may hold values from 0 to 31
Outputs:
- density: float32 [768, 128], P('vir')
- grad: float32 [96, 768, 128], P('tri', 'vir')
The draws below stay inside these ranges and needn't reach their ends.
Inputs may be any that keep to these rules, and one draw needn't show every extreme that they name: `block_sizes`: block sizes sum to 64; at least one block has exactly 3 orbitals. `roots`: each tri index stores exactly one block. `triples`: block numbers; a pair may repeat a block.
All inputs are finite; a program needn't handle non-finite values.
Results may differ from the reference program's by a relative error of at most 0.0003.
Values may be sent and summed in bfloat16 or wider, within the bound.
No kernel may reach another device: no remote copies, remote signals or barrier semaphores. Data moves between devices by JAX's collectives and lax.ppermute only.
A program may use at most 64 MiB of HBM per device.

```python
import math
import jax
import jax.numpy as jnp
import numpy as np
from jax import lax

NV = 768
NB = 128
BMAX = 3
TPO = 12
NOCC = 64
N_TRI = 32


def with_ends(result, stream_key, low, largest):
    shape = result.shape
    place = [jax.random.randint(jax.random.fold_in(stream_key, axis), (), 0, shape[axis]) for axis in range(len(shape))]
    result = result.at[tuple(place)].set(low)
    longest = shape.index(max(shape))
    place[longest] = (place[longest] + 1) % shape[longest]
    return result.at[tuple(place)].set(largest)


def block_scale(stream_key, dims, cuts, low, top_value):
    level = 1.0
    for dim, blocks in cuts:
        steps = jax.random.uniform(jax.random.fold_in(jax.random.fold_in(stream_key, 6), dim), (blocks,), jnp.float32, low / len(cuts), top_value / len(cuts))
        level = level * jnp.repeat(jnp.exp(steps), dims[dim] // blocks).reshape((-1,) + (1,) * (len(dims) - 1 - dim))
    return level


def split_up(amount, total, limit, skew):
    loads = [(1 << 20) // math.isqrt(rank ** skew) + 1 for rank in range(2, amount + 1)]
    surplus, holding = total - limit - (amount - 1), [1] * (amount - 1)
    while surplus > 0:
        movable = [i for i in range(amount - 1) if holding[i] < limit]
        pool, budget = sum([loads[i] for i in movable]), surplus
        for i in movable:
            extra = min(limit - holding[i], max(1, budget * loads[i] // pool), surplus)
            holding[i] = holding[i] + extra
            surplus = surplus - extra
    return np.array([limit] + holding)


def uneven_parts(stream_key, count, total, limit, lean):
    if count == 2:
        one = jax.random.randint(stream_key, (), max(1, total - limit), min(limit, total - 1) + 1)
        return jnp.stack([one, total - one])
    sizes = jnp.asarray(split_up(count, total, limit, lean), jnp.int32)
    couples = (count - 1) // 2
    donor, taker = sizes[1:1 + 2 * couples:2], sizes[2:2 + 2 * couples:2]
    slack = jnp.minimum(donor - 1, limit - taker)
    passed = jax.random.randint(jax.random.fold_in(stream_key, 1), (couples,), 0, 1 << 20) % (slack + 1)
    sizes = sizes.at[1:1 + 2 * couples:2].set(donor - passed).at[2:2 + 2 * couples:2].set(taker + passed)
    return sizes[jax.random.permutation(jax.random.fold_in(stream_key, 2), count)]


def bell_draw(stream_key, dims, scale, most, pieces=(), kind=jnp.bfloat16):
    entries = scale * jax.random.normal(stream_key, dims, jnp.float32)
    if pieces:
        entries = entries * block_scale(stream_key, dims, pieces, -0.22, 0.18)
    return jnp.clip(entries, -most, most).astype(kind)


def setup_inputs(seed: int = 0) -> dict:
    streams_of = jax.random.split(jax.random.key(seed), 9)
    amps = bell_draw(streams_of[0], (N_TRI * BMAX, NV, NV), NV ** -0.5, 0.21875, ((0, 32), (1, 16)))
    vvvo = bell_draw(streams_of[1], (N_TRI * BMAX, NV, NB), 1.0, 6.0, ((0, 32), (1, 16)))
    occ_gap = jnp.clip(jax.random.uniform(streams_of[2], (NOCC,), jnp.float32, 0.3, 1.0), 0.3, 1.0)
    vir_gap = jnp.clip(0.5 + 1.5 * jax.random.uniform(streams_of[3], (NV,), jnp.float32) ** block_scale(streams_of[3], (NV,), ((0, 16),), -0.2, 0.2), 0.5, 2.0)
    pair_gap = jnp.clip(jax.random.uniform(streams_of[4], (NB,), jnp.float32, 0.5, 2.0), 0.5, 2.0)
    block_sizes = uneven_parts(streams_of[5], N_TRI, NOCC, BMAX, 2).astype(jnp.int32)
    roots = jax.random.permutation(streams_of[6], N_TRI).astype(jnp.int32)
    triples = with_ends(jax.random.randint(streams_of[7], (N_TRI * TPO, 2), 0, N_TRI), jax.random.fold_in(streams_of[7], 1), 0, N_TRI - 1).astype(jnp.int32)
    return dict(amps=amps, vvvo=vvvo, occ_gap=occ_gap, vir_gap=vir_gap, pair_gap=pair_gap, block_sizes=block_sizes, roots=roots, triples=triples)


def reference(amps, vvvo, occ_gap, vir_gap, pair_gap, block_sizes, roots, triples):
    slot_ids = jnp.arange(BMAX, dtype=jnp.int32)
    offsets = (jnp.cumsum(block_sizes) - block_sizes).astype(jnp.int32)
    owned = jnp.argsort(roots).astype(jnp.int32)

    def owner_step(density, owner_index):
        kblock = owned[owner_index]
        integral_values = lax.dynamic_slice_in_dim(vvvo, (owner_index * BMAX).astype(jnp.int32), BMAX, 0).astype(jnp.float32)
        own_gaps = occ_gap[jnp.minimum(offsets[kblock] + slot_ids, NOCC - 1)]
        own_live = slot_ids < block_sizes[kblock]
        base_den = vir_gap[:, None, None] + own_gaps[None, :, None] + pair_gap[None, None, :]
        pair_rows = lax.dynamic_slice_in_dim(triples, (owner_index * TPO).astype(jnp.int32), TPO, 0)

        def one_pair(state, pair_row):
            density_acc, gradient_running_total = state
            integral_layers = []
            projected_block = []
            gap_values = []
            live_masks = []
            for which_side in range(2):
                block_id = pair_row[which_side]
                row_ids = roots[block_id] * BMAX + slot_ids
                amplitude_layer = jnp.take(amps, row_ids, axis=0).astype(jnp.float32)
                integral_layers.append(amplitude_layer)
                projected_block.append(jnp.einsum('flg,ugw->fluw', amplitude_layer, integral_values))
                gap_values.append(occ_gap[jnp.minimum(offsets[block_id] + slot_ids, NOCC - 1)])
                live_masks.append(slot_ids < block_sizes[block_id])
            full_den = base_den[None, None] + gap_values[0][:, None, None, None, None] + gap_values[1][None, :, None, None, None]
            live_mask = live_masks[0][:, None, None, None, None] & live_masks[1][None, :, None, None, None] & own_live[None, None, None, :, None]
            weighted = jnp.where(live_mask, projected_block[0][:, None] * projected_block[1][None] / full_den, 0.0)
            density_acc = density_acc + jnp.sum(weighted * weighted, axis=(0, 1, 3))
            gradient_running_total = gradient_running_total + jnp.einsum('rnw,rqnhe->hwe', integral_layers[0], weighted, precision=lax.Precision.HIGHEST)
            return (density_acc, gradient_running_total), None

        start_grad = jnp.zeros((BMAX, NV, NB), jnp.float32)
        (density, grad_rows), _ = lax.scan(one_pair, (density, start_grad), pair_rows)
        return density, grad_rows

    start_density = jnp.zeros((NV, NB), jnp.float32)
    density, grad_all = lax.scan(owner_step, start_density, jnp.arange(N_TRI, dtype=jnp.int32))
    density = density / float(N_TRI * TPO)
    return density, grad_all.reshape(N_TRI * BMAX, NV, NB)
```

```python
import jax
import jax.numpy as jnp
from jax import lax
from jax.sharding import PartitionSpec as P

BMAX = 3


def body(amps, vvvo, occ_gap, vir_gap, pair_gap, block_sizes, roots, triples):
    tri_count = lax.axis_size("tri")
    me = lax.axis_index("tri")
    npair = triples.shape[0]
    nocc = occ_gap.shape[0]
    nrow = tri_count * BMAX
    f32, bf16 = jnp.float32, jnp.bfloat16
    slots = jnp.arange(BMAX, dtype=jnp.int32)
    offsets = (jnp.cumsum(block_sizes) - block_sizes).astype(jnp.int32)

    own = roots == me
    own_size = jnp.sum(jnp.where(own, block_sizes, 0))
    own_off = jnp.sum(jnp.where(own, offsets, 0))
    own_gap = occ_gap[jnp.minimum(own_off + slots, nocc - 1)]
    own_live = slots < own_size

    pair_root = roots[triples]
    pair_gap_occ = occ_gap[jnp.minimum(offsets[triples][..., None] + slots, nocc - 1)]
    pair_live = slots < block_sizes[triples][..., None]
    rows = pair_root[..., None] * BMAX + slots

    everything = lax.all_gather(amps, "tri", axis=0, tiled=True)
    table = lax.all_gather(vvvo, "vir", axis=1, tiled=True)

    pick = (rows.reshape(-1)[:, None] == jnp.arange(nrow, dtype=jnp.int32)).astype(bf16)
    picked = jnp.einsum("rb,bad->rad", pick, everything, preferred_element_type=bf16)
    proj = jnp.einsum("rad,kdm->rakm", picked, table, preferred_element_type=f32)
    nv, nk, nm = proj.shape[1], proj.shape[2], proj.shape[3]
    proj = proj.reshape(npair, 2, BMAX, nv, nk, nm)
    left, right = proj[:, 0], proj[:, 1]

    base = vir_gap[:, None, None] + own_gap[None, :, None] + pair_gap[None, None, :]
    den = (
        base[None, None, None]
        + pair_gap_occ[:, 0, :, None, None, None, None]
        + pair_gap_occ[:, 1, None, :, None, None, None]
    )
    live = (
        pair_live[:, 0, :, None, None, None, None]
        & pair_live[:, 1, None, :, None, None, None]
        & own_live[None, None, None, None, :, None]
    )
    weighted = jnp.where(live, left[:, :, None] * right[:, None] / den, 0.0)
    dens_part = jnp.sum(weighted * weighted, axis=(0, 1, 2, 4))
    summed = jnp.sum(weighted, axis=2)

    hi_f32 = lax.reduce_precision(summed, exponent_bits=8, mantissa_bits=7)
    hi = hi_f32.astype(bf16)
    lo = (summed - hi_f32).astype(bf16)
    left_rows = picked.reshape(npair, 2, BMAX, nv, -1)[:, 0]
    grad = jnp.einsum("qiad,qiakm->dkm", left_rows, hi, preferred_element_type=f32)
    grad = grad + jnp.einsum("qiad,qiakm->dkm", left_rows, lo, preferred_element_type=f32)
    grad = lax.psum_scatter(grad, "vir", scatter_dimension=0, tiled=True)
    grad = jnp.transpose(grad, (1, 0, 2))

    density = lax.psum(dens_part, "tri") / float(tri_count * npair)
    return density, grad


def solution(mesh):
    return jax.shard_map(
        body,
        mesh=mesh,
        in_specs=(
            P("tri", "vir", None),
            P("tri", "vir", None),
            P(),
            P("vir"),
            P(),
            P(),
            P(),
            P("tri", None),
        ),
        out_specs=(P("vir", None), P("tri", "vir", None)),
        check_vma=False,
    )
```

```python
import jax
import jax.numpy as jnp
from jax import lax
from jax.sharding import Mesh
from jax.sharding import PartitionSpec as P

BMAX = 3
TRI = ("tri_0", "tri_1")


def whole_of(x, axes, dim):
    if not axes:
        return x
    nearer = lax.all_gather(x, axes[-1], axis=dim, tiled=True)
    return whole_of(nearer, axes[:-1], dim)


def from_everyone(x, axis):
    copies = jnp.broadcast_to(x, (lax.axis_size(axis), *x.shape))
    return lax.all_to_all(copies, axis, split_axis=0, concat_axis=0, tiled=True)


def joined_along(pieces, dim):
    pieces = jnp.moveaxis(pieces, 0, dim)
    lengths = pieces.shape
    return pieces.reshape(*lengths[:dim], lengths[dim] * lengths[dim + 1], *lengths[dim + 2 :])


def sent_and_summed(x, axis, dim):
    before, after = (x.shape[:dim], x.shape[dim + 1 :])
    pieces = jnp.moveaxis(x.reshape(*before, lax.axis_size(axis), -1, *after), dim, 0)
    arrived = lax.all_to_all(pieces, axis, split_axis=0, concat_axis=0, tiled=True)
    return arrived.sum(axis=0)


def butterfly_sum(x, axes):
    count = lax.axis_size(axes)
    bit = 1
    while bit < count:
        perm = [(i, i ^ bit) for i in range(count)]
        x = x + lax.ppermute(x, axes, perm)
        bit *= 2
    return x


def body(amps, vvvo, occ_gap, vir_gap, pair_gap, block_sizes, roots, triples):
    tri_count = lax.axis_size(TRI)
    me = lax.axis_index(TRI)
    npair = triples.shape[0]
    nocc = occ_gap.shape[0]
    nrow = tri_count * BMAX
    f32, bf16 = jnp.float32, jnp.bfloat16
    slots = jnp.arange(BMAX, dtype=jnp.int32)
    offsets = (jnp.cumsum(block_sizes) - block_sizes).astype(jnp.int32)

    own = roots == me
    own_size = jnp.sum(jnp.where(own, block_sizes, 0))
    own_off = jnp.sum(jnp.where(own, offsets, 0))
    own_gap = occ_gap[jnp.minimum(own_off + slots, nocc - 1)]
    own_live = slots < own_size

    pair_root = roots[triples]
    pair_gap_occ = occ_gap[jnp.minimum(offsets[triples][..., None] + slots, nocc - 1)]
    pair_live = slots < block_sizes[triples][..., None]
    rows = pair_root[..., None] * BMAX + slots

    everything = whole_of(amps, TRI, 0)
    table = joined_along(from_everyone(vvvo, "vir"), 1)

    pick = (rows.reshape(-1)[:, None] == jnp.arange(nrow, dtype=jnp.int32)).astype(bf16)
    picked = jnp.einsum("rb,bad->rad", pick, everything, preferred_element_type=bf16)
    proj = jnp.einsum("rad,kdm->rakm", picked, table, preferred_element_type=f32)
    nv, nk, nm = proj.shape[1], proj.shape[2], proj.shape[3]
    proj = proj.reshape(npair, 2, BMAX, nv, nk, nm)
    left, right = proj[:, 0], proj[:, 1]

    base = vir_gap[:, None, None] + own_gap[None, :, None] + pair_gap[None, None, :]
    den = (
        base[None, None, None]
        + pair_gap_occ[:, 0, :, None, None, None, None]
        + pair_gap_occ[:, 1, None, :, None, None, None]
    )
    live = (
        pair_live[:, 0, :, None, None, None, None]
        & pair_live[:, 1, None, :, None, None, None]
        & own_live[None, None, None, None, :, None]
    )
    weighted = jnp.where(live, left[:, :, None] * right[:, None] / den, 0.0)
    dens_part = jnp.sum(weighted * weighted, axis=(0, 1, 2, 4))
    summed = jnp.sum(weighted, axis=2)

    hi_f32 = lax.reduce_precision(summed, exponent_bits=8, mantissa_bits=7)
    hi = hi_f32.astype(bf16)
    lo = (summed - hi_f32).astype(bf16)
    left_rows = picked.reshape(npair, 2, BMAX, nv, -1)[:, 0]
    grad = jnp.einsum("qiad,qiakm->dkm", left_rows, hi, preferred_element_type=f32)
    grad = grad + jnp.einsum("qiad,qiakm->dkm", left_rows, lo, preferred_element_type=f32)
    grad = sent_and_summed(grad, "vir", 0)
    grad = jnp.transpose(grad, (1, 0, 2))

    density = butterfly_sum(dens_part, TRI) / float(tri_count * npair)
    return density, grad


def solution(mesh):
    tri_hi = mesh.shape["tri"] // 4
    finer = Mesh(mesh.devices.reshape(tri_hi, 4, mesh.shape["vir"]), ("tri_0", "tri_1", "vir"))
    return jax.shard_map(
        body,
        mesh=finer,
        in_specs=(
            P(TRI, "vir", None),
            P(TRI, "vir", None),
            P(),
            P("vir"),
            P(),
            P(),
            P(),
            P(TRI, None),
        ),
        out_specs=(P("vir", None), P(TRI, "vir", None)),
        check_vma=False,
    )
```

```python
import jax
import jax.numpy as jnp
from jax import lax
from jax.sharding import Mesh
from jax.sharding import PartitionSpec as P

BMAX = 3
TRI = ("tri_0", "tri_1")


def whole_of(x, axes, dim):
    if not axes:
        return x
    nearer = lax.all_gather(x, axes[-1], axis=dim, tiled=True)
    return whole_of(nearer, axes[:-1], dim)


def from_everyone(x, axis):
    copies = jnp.broadcast_to(x, (lax.axis_size(axis), *x.shape))
    return lax.all_to_all(copies, axis, split_axis=0, concat_axis=0, tiled=True)


def joined_along(pieces, dim):
    pieces = jnp.moveaxis(pieces, 0, dim)
    lengths = pieces.shape
    return pieces.reshape(*lengths[:dim], lengths[dim] * lengths[dim + 1], *lengths[dim + 2 :])


def sent_and_summed(x, axis, dim):
    before, after = (x.shape[:dim], x.shape[dim + 1 :])
    pieces = jnp.moveaxis(x.reshape(*before, lax.axis_size(axis), -1, *after), dim, 0)
    arrived = lax.all_to_all(pieces, axis, split_axis=0, concat_axis=0, tiled=True)
    return arrived.sum(axis=0)


def reduce_tails(grad, dens, vir_bits, tri_bits):
    vir_count = lax.axis_size("vir")
    tri_count = lax.axis_size(TRI)
    nbits = vir_count.bit_length() - 1
    me = lax.axis_index("vir")
    grad = grad.reshape((2,) * nbits + grad.shape[1:])
    for r in range(max(len(vir_bits), len(tri_bits))):
        if r < len(vir_bits):
            bit = vir_bits[r]
            dim = nbits - 1 - bit
            mine = (me >> bit) & 1
            keep = lax.dynamic_index_in_dim(grad, mine, axis=dim, keepdims=True)
            send = lax.dynamic_index_in_dim(grad, 1 - mine, axis=dim, keepdims=True)
            perm = [(i, i ^ (1 << bit)) for i in range(vir_count)]
            grad = keep + lax.ppermute(send, "vir", perm)
        if r < len(tri_bits):
            bit = tri_bits[r]
            perm = [(i, i ^ (1 << bit)) for i in range(tri_count)]
            dens = dens + lax.ppermute(dens, TRI, perm)
    return grad.reshape(grad.shape[nbits:]), dens


def butterfly_sum(x, axes):
    count = lax.axis_size(axes)
    bit = 1
    while bit < count:
        perm = [(i, i ^ bit) for i in range(count)]
        x = x + lax.ppermute(x, axes, perm)
        bit *= 2
    return x


def body(amps, vvvo, occ_gap, vir_gap, pair_gap, block_sizes, roots, triples):
    tri_count = lax.axis_size(TRI)
    me = lax.axis_index(TRI)
    npair = triples.shape[0]
    nocc = occ_gap.shape[0]
    nrow = tri_count * BMAX
    f32, bf16 = jnp.float32, jnp.bfloat16
    slots = jnp.arange(BMAX, dtype=jnp.int32)
    offsets = (jnp.cumsum(block_sizes) - block_sizes).astype(jnp.int32)

    own = roots == me
    own_size = jnp.sum(jnp.where(own, block_sizes, 0))
    own_off = jnp.sum(jnp.where(own, offsets, 0))
    own_gap = occ_gap[jnp.minimum(own_off + slots, nocc - 1)]
    own_live = slots < own_size

    pair_root = roots[triples]
    pair_gap_occ = occ_gap[jnp.minimum(offsets[triples][..., None] + slots, nocc - 1)]
    pair_live = slots < block_sizes[triples][..., None]
    rows = pair_root[..., None] * BMAX + slots

    everything = whole_of(amps, TRI, 0)
    table = joined_along(from_everyone(vvvo, "vir"), 1)

    pick = (rows.reshape(-1)[:, None] == jnp.arange(nrow, dtype=jnp.int32)).astype(bf16)
    picked = jnp.einsum("rb,bad->rad", pick, everything, preferred_element_type=bf16)
    proj = jnp.einsum("rad,kdm->rakm", picked, table, preferred_element_type=f32)
    nv, nk, nm = proj.shape[1], proj.shape[2], proj.shape[3]
    proj = proj.reshape(npair, 2, BMAX, nv, nk, nm)
    left, right = proj[:, 0], proj[:, 1]

    base = vir_gap[:, None, None] + own_gap[None, :, None] + pair_gap[None, None, :]
    den = (
        base[None, None, None]
        + pair_gap_occ[:, 0, :, None, None, None, None]
        + pair_gap_occ[:, 1, None, :, None, None, None]
    )
    live = (
        pair_live[:, 0, :, None, None, None, None]
        & pair_live[:, 1, None, :, None, None, None]
        & own_live[None, None, None, None, :, None]
    )
    weighted = jnp.where(live, left[:, :, None] * right[:, None] / den, 0.0)
    dens_part = jnp.sum(weighted * weighted, axis=(0, 1, 2, 4))
    summed = jnp.sum(weighted, axis=2)

    hi_f32 = lax.reduce_precision(summed, exponent_bits=8, mantissa_bits=7)
    hi = hi_f32.astype(bf16)
    lo = (summed - hi_f32).astype(bf16)
    left_rows = picked.reshape(npair, 2, BMAX, nv, -1)[:, 0]
    grad = jnp.einsum("qiad,qiakm->dkm", left_rows, hi, preferred_element_type=f32)
    grad = grad + jnp.einsum("qiad,qiakm->dkm", left_rows, lo, preferred_element_type=f32)
    vir_count = lax.axis_size("vir")
    grad = grad.reshape(vir_count, -1, grad.shape[1], grad.shape[2])
    grad, density = reduce_tails(grad, dens_part, (0, 2, 3, 1), (0, 1, 2, 3, 4))
    grad = jnp.transpose(grad, (1, 0, 2))
    density = density / float(tri_count * npair)
    return density, grad


def solution(mesh):
    tri_hi = mesh.shape["tri"] // 4
    finer = Mesh(mesh.devices.reshape(tri_hi, 4, mesh.shape["vir"]), ("tri_0", "tri_1", "vir"))
    return jax.shard_map(
        body,
        mesh=finer,
        in_specs=(
            P(TRI, "vir", None),
            P(TRI, "vir", None),
            P(),
            P("vir"),
            P(),
            P(),
            P(),
            P(TRI, None),
        ),
        out_specs=(P("vir", None), P(TRI, "vir", None)),
        check_vma=False,
    )
```

```python
import jax
import jax.numpy as jnp
from jax import lax
from jax.sharding import Mesh
from jax.sharding import PartitionSpec as P

BMAX = 3
TRI = ("tri_0", "tri_1")


def whole_of(x, axes, dim):
    if not axes:
        return x
    nearer = lax.all_gather(x, axes[-1], axis=dim, tiled=True)
    return whole_of(nearer, axes[:-1], dim)


def from_everyone(x, axis):
    copies = jnp.broadcast_to(x, (lax.axis_size(axis), *x.shape))
    return lax.all_to_all(copies, axis, split_axis=0, concat_axis=0, tiled=True)


def joined_along(pieces, dim):
    pieces = jnp.moveaxis(pieces, 0, dim)
    lengths = pieces.shape
    return pieces.reshape(*lengths[:dim], lengths[dim] * lengths[dim + 1], *lengths[dim + 2 :])


def sent_and_summed(x, axis, dim):
    before, after = (x.shape[:dim], x.shape[dim + 1 :])
    pieces = jnp.moveaxis(x.reshape(*before, lax.axis_size(axis), -1, *after), dim, 0)
    arrived = lax.all_to_all(pieces, axis, split_axis=0, concat_axis=0, tiled=True)
    return arrived.sum(axis=0)


def reduce_tails(grad, dens, vir_bits, tri_bits):
    vir_count = lax.axis_size("vir")
    tri_count = lax.axis_size(TRI)
    nbits = vir_count.bit_length() - 1
    me = lax.axis_index("vir")
    grad = grad.reshape((2,) * nbits + grad.shape[1:])
    for r in range(max(len(vir_bits), len(tri_bits))):
        if r < len(vir_bits):
            bit = vir_bits[r]
            dim = nbits - 1 - bit
            mine = (me >> bit) & 1
            keep = lax.dynamic_index_in_dim(grad, mine, axis=dim, keepdims=True)
            send = lax.dynamic_index_in_dim(grad, 1 - mine, axis=dim, keepdims=True)
            perm = [(i, i ^ (1 << bit)) for i in range(vir_count)]
            grad = keep + lax.ppermute(send, "vir", perm)
        if r < len(tri_bits):
            bit = tri_bits[r]
            perm = [(i, i ^ (1 << bit)) for i in range(tri_count)]
            dens = dens + lax.ppermute(dens, TRI, perm)
    return grad.reshape(grad.shape[nbits:]), dens


def butterfly_sum(x, axes):
    count = lax.axis_size(axes)
    bit = 1
    while bit < count:
        perm = [(i, i ^ bit) for i in range(count)]
        x = x + lax.ppermute(x, axes, perm)
        bit *= 2
    return x


def body(amps, vvvo, occ_gap, vir_gap, pair_gap, block_sizes, roots, triples):
    tri_count = lax.axis_size(TRI)
    me = lax.axis_index(TRI)
    npair = triples.shape[0]
    nocc = occ_gap.shape[0]
    nrow = tri_count * BMAX
    f32, bf16 = jnp.float32, jnp.bfloat16
    slots = jnp.arange(BMAX, dtype=jnp.int32)
    offsets = (jnp.cumsum(block_sizes) - block_sizes).astype(jnp.int32)

    own = roots == me
    own_size = jnp.sum(jnp.where(own, block_sizes, 0))
    own_off = jnp.sum(jnp.where(own, offsets, 0))
    own_gap = occ_gap[jnp.minimum(own_off + slots, nocc - 1)]
    own_live = slots < own_size

    pair_root = roots[triples]
    pair_gap_occ = occ_gap[jnp.minimum(offsets[triples][..., None] + slots, nocc - 1)]
    pair_live = slots < block_sizes[triples][..., None]
    rows = pair_root[..., None] * BMAX + slots

    split = (amps.shape[2] * 2) // 3
    first_half = whole_of(amps[:, :, :split], TRI, 0)
    across = lax.all_gather(amps[:, :, split:], "tri_0", axis=0, tiled=True)
    second_half = joined_along(from_everyone(across, "tri_1"), 0)
    table = joined_along(from_everyone(vvvo, "vir"), 1)

    tri_lo = lax.axis_size("tri_1")
    tri_hi = lax.axis_size("tri_0")
    flat_rows = rows.reshape(-1)
    swapped_rows = (
        (pair_root % tri_lo)[..., None] * (tri_hi * BMAX) + (pair_root // tri_lo)[..., None] * BMAX + slots
    ).reshape(-1)
    row_ids = jnp.arange(nrow, dtype=jnp.int32)
    pick_a = (flat_rows[:, None] == row_ids).astype(bf16)
    pick_b = (swapped_rows[:, None] == row_ids).astype(bf16)
    picked_a = jnp.einsum("rb,bad->rad", pick_a, first_half, preferred_element_type=bf16)
    picked_b = jnp.einsum("rb,bad->rad", pick_b, second_half, preferred_element_type=bf16)
    proj = jnp.einsum("rad,kdm->rakm", picked_a, table[:, :split], preferred_element_type=f32)
    proj = proj + jnp.einsum("rad,kdm->rakm", picked_b, table[:, split:], preferred_element_type=f32)
    nv, nk, nm = proj.shape[1], proj.shape[2], proj.shape[3]
    proj = proj.reshape(npair, 2, BMAX, nv, nk, nm)
    left, right = proj[:, 0], proj[:, 1]

    base = vir_gap[:, None, None] + own_gap[None, :, None] + pair_gap[None, None, :]
    den = (
        base[None, None, None]
        + pair_gap_occ[:, 0, :, None, None, None, None]
        + pair_gap_occ[:, 1, None, :, None, None, None]
    )
    live = (
        pair_live[:, 0, :, None, None, None, None]
        & pair_live[:, 1, None, :, None, None, None]
        & own_live[None, None, None, None, :, None]
    )
    weighted = jnp.where(live, left[:, :, None] * right[:, None] / den, 0.0)
    dens_part = jnp.sum(weighted * weighted, axis=(0, 1, 2, 4))
    summed = jnp.sum(weighted, axis=2)

    hi_f32 = lax.reduce_precision(summed, exponent_bits=8, mantissa_bits=7)
    hi = hi_f32.astype(bf16)
    lo = (summed - hi_f32).astype(bf16)
    def grad_of(picked):
        left_rows = picked.reshape(npair, 2, BMAX, nv, -1)[:, 0]
        g = jnp.einsum("qiad,qiakm->dkm", left_rows, hi, preferred_element_type=f32)
        return g + jnp.einsum("qiad,qiakm->dkm", left_rows, lo, preferred_element_type=f32)

    grad = jnp.concatenate([grad_of(picked_a), grad_of(picked_b)], axis=0)
    vir_count = lax.axis_size("vir")
    grad = grad.reshape(vir_count, -1, grad.shape[1], grad.shape[2])
    grad, density = reduce_tails(grad, dens_part, (0, 2, 3, 1), (0, 1, 2, 3, 4))
    grad = jnp.transpose(grad, (1, 0, 2))
    density = density / float(tri_count * npair)
    return density, grad


def solution(mesh):
    tri_hi = mesh.shape["tri"] // 4
    finer = Mesh(mesh.devices.reshape(tri_hi, 4, mesh.shape["vir"]), ("tri_0", "tri_1", "vir"))
    return jax.shard_map(
        body,
        mesh=finer,
        in_specs=(
            P(TRI, "vir", None),
            P(TRI, "vir", None),
            P(),
            P("vir"),
            P(),
            P(),
            P(),
            P(TRI, None),
        ),
        out_specs=(P("vir", None), P(TRI, "vir", None)),
        check_vma=False,
    )
```

```python
import jax
import jax.numpy as jnp
from jax import lax
from jax.sharding import Mesh
from jax.sharding import PartitionSpec as P

BMAX = 3
TRI = ("tri_0", "tri_1")


def whole_of(x, axes, dim):
    if not axes:
        return x
    nearer = lax.all_gather(x, axes[-1], axis=dim, tiled=True)
    return whole_of(nearer, axes[:-1], dim)


def from_everyone(x, axis):
    copies = jnp.broadcast_to(x, (lax.axis_size(axis), *x.shape))
    return lax.all_to_all(copies, axis, split_axis=0, concat_axis=0, tiled=True)


def joined_along(pieces, dim):
    pieces = jnp.moveaxis(pieces, 0, dim)
    lengths = pieces.shape
    return pieces.reshape(*lengths[:dim], lengths[dim] * lengths[dim + 1], *lengths[dim + 2 :])


def sent_and_summed(x, axis, dim):
    before, after = (x.shape[:dim], x.shape[dim + 1 :])
    pieces = jnp.moveaxis(x.reshape(*before, lax.axis_size(axis), -1, *after), dim, 0)
    arrived = lax.all_to_all(pieces, axis, split_axis=0, concat_axis=0, tiled=True)
    return arrived.sum(axis=0)


def reduce_tails(grad, dens, vir_bits, tri_bits):
    vir_count = lax.axis_size("vir")
    tri_count = lax.axis_size(TRI)
    nbits = vir_count.bit_length() - 1
    me = lax.axis_index("vir")
    grad = grad.reshape((2,) * nbits + grad.shape[1:])
    for r in range(max(len(vir_bits), len(tri_bits))):
        if r < len(vir_bits):
            bit = vir_bits[r]
            dim = nbits - 1 - bit
            mine = (me >> bit) & 1
            keep = lax.dynamic_index_in_dim(grad, mine, axis=dim, keepdims=True)
            send = lax.dynamic_index_in_dim(grad, 1 - mine, axis=dim, keepdims=True)
            perm = [(i, i ^ (1 << bit)) for i in range(vir_count)]
            grad = keep + lax.ppermute(send, "vir", perm)
        if r < len(tri_bits):
            bit = tri_bits[r]
            perm = [(i, i ^ (1 << bit)) for i in range(tri_count)]
            dens = dens + lax.ppermute(dens, TRI, perm)
    return grad.reshape(grad.shape[nbits:]), dens


def butterfly_sum(x, axes):
    count = lax.axis_size(axes)
    bit = 1
    while bit < count:
        perm = [(i, i ^ bit) for i in range(count)]
        x = x + lax.ppermute(x, axes, perm)
        bit *= 2
    return x


def body(amps, vvvo, occ_gap, vir_gap, pair_gap, block_sizes, roots, triples):
    tri_count = lax.axis_size(TRI)
    me = lax.axis_index(TRI)
    npair = triples.shape[0]
    nocc = occ_gap.shape[0]
    nrow = tri_count * BMAX
    f32, bf16 = jnp.float32, jnp.bfloat16
    slots = jnp.arange(BMAX, dtype=jnp.int32)
    offsets = (jnp.cumsum(block_sizes) - block_sizes).astype(jnp.int32)

    own = roots == me
    own_size = jnp.sum(jnp.where(own, block_sizes, 0))
    own_off = jnp.sum(jnp.where(own, offsets, 0))
    own_gap = occ_gap[jnp.minimum(own_off + slots, nocc - 1)]
    own_live = slots < own_size

    pair_root = roots[triples]
    pair_gap_occ = occ_gap[jnp.minimum(offsets[triples][..., None] + slots, nocc - 1)]
    pair_live = slots < block_sizes[triples][..., None]
    rows = pair_root[..., None] * BMAX + slots

    split = amps.shape[2] // 2
    first_half = whole_of(amps[:, :, :split], TRI, 0)
    second_half = whole_of(amps[:, :, split:], TRI, 0)
    table = joined_along(from_everyone(vvvo, "vir"), 1)

    pick = (rows.reshape(-1)[:, None] == jnp.arange(nrow, dtype=jnp.int32)).astype(bf16)
    picked_a = jnp.einsum("rb,bad->rad", pick, first_half, preferred_element_type=bf16)
    picked_b = jnp.einsum("rb,bad->rad", pick, second_half, preferred_element_type=bf16)
    proj = jnp.einsum("rad,kdm->rakm", picked_a, table[:, :split], preferred_element_type=f32)
    proj = proj + jnp.einsum("rad,kdm->rakm", picked_b, table[:, split:], preferred_element_type=f32)
    nv, nk, nm = proj.shape[1], proj.shape[2], proj.shape[3]
    proj = proj.reshape(npair, 2, BMAX, nv, nk, nm)
    left, right = proj[:, 0], proj[:, 1]

    base = vir_gap[:, None, None] + own_gap[None, :, None] + pair_gap[None, None, :]
    den = (
        base[None, None, None]
        + pair_gap_occ[:, 0, :, None, None, None, None]
        + pair_gap_occ[:, 1, None, :, None, None, None]
    )
    live = (
        pair_live[:, 0, :, None, None, None, None]
        & pair_live[:, 1, None, :, None, None, None]
        & own_live[None, None, None, None, :, None]
    )
    weighted = jnp.where(live, left[:, :, None] * right[:, None] / den, 0.0)
    dens_part = jnp.sum(weighted * weighted, axis=(0, 1, 2, 4))
    summed = jnp.sum(weighted, axis=2)

    hi_f32 = lax.reduce_precision(summed, exponent_bits=8, mantissa_bits=7)
    hi = hi_f32.astype(bf16)
    lo = (summed - hi_f32).astype(bf16)
    def grad_of(picked):
        left_rows = picked.reshape(npair, 2, BMAX, nv, -1)[:, 0]
        g = jnp.einsum("qiad,qiakm->dkm", left_rows, hi, preferred_element_type=f32)
        return g + jnp.einsum("qiad,qiakm->dkm", left_rows, lo, preferred_element_type=f32)

    grad = jnp.concatenate([grad_of(picked_a), grad_of(picked_b)], axis=0)
    vir_count = lax.axis_size("vir")
    grad = grad.reshape(vir_count, -1, grad.shape[1], grad.shape[2])
    grad, density = reduce_tails(grad, dens_part, (0, 2, 3, 1), (0, 1, 2, 3, 4))
    grad = jnp.transpose(grad, (1, 0, 2))
    density = density / float(tri_count * npair)
    return density, grad


def solution(mesh):
    tri_hi = mesh.shape["tri"] // 4
    finer = Mesh(mesh.devices.reshape(tri_hi, 4, mesh.shape["vir"]), ("tri_0", "tri_1", "vir"))
    return jax.shard_map(
        body,
        mesh=finer,
        in_specs=(
            P(TRI, "vir", None),
            P(TRI, "vir", None),
            P(),
            P("vir"),
            P(),
            P(),
            P(),
            P(TRI, None),
        ),
        out_specs=(P("vir", None), P(TRI, "vir", None)),
        check_vma=False,
    )
```

```python
import jax
import jax.numpy as jnp
from jax import lax
from jax.sharding import Mesh
from jax.sharding import PartitionSpec as P

BMAX = 3
TRI = ("tri_0", "tri_1")
VIR = ("vx", "vz", "vc")


def whole_of(x, axes, dim):
    if not axes:
        return x
    nearer = lax.all_gather(x, axes[-1], axis=dim, tiled=True)
    return whole_of(nearer, axes[:-1], dim)


def from_everyone(x, axis):
    copies = jnp.broadcast_to(x, (lax.axis_size(axis), *x.shape))
    return lax.all_to_all(copies, axis, split_axis=0, concat_axis=0, tiled=True)


def joined_along(pieces, dim):
    pieces = jnp.moveaxis(pieces, 0, dim)
    lengths = pieces.shape
    return pieces.reshape(*lengths[:dim], lengths[dim] * lengths[dim + 1], *lengths[dim + 2 :])


def sent_and_summed(x, axis, dim):
    before, after = (x.shape[:dim], x.shape[dim + 1 :])
    pieces = jnp.moveaxis(x.reshape(*before, lax.axis_size(axis), -1, *after), dim, 0)
    arrived = lax.all_to_all(pieces, axis, split_axis=0, concat_axis=0, tiled=True)
    return arrived.sum(axis=0)


def halve(x, axis, dim):
    mine = lax.axis_index(axis)
    keep = lax.dynamic_index_in_dim(x, mine, axis=dim, keepdims=False)
    send = lax.dynamic_index_in_dim(x, 1 - mine, axis=dim, keepdims=False)
    return keep + lax.ppermute(send, axis, [(0, 1), (1, 0)])


def reduce_tails(grad, dens, tri_bits):
    tri_count = lax.axis_size(TRI)
    grad = halve(grad, "vc", 2)
    for r, bit in enumerate(tri_bits):
        perm = [(i, i ^ (1 << bit)) for i in range(tri_count)]
        dens = dens + lax.ppermute(dens, TRI, perm)
        if r == 0:
            grad = lax.psum_scatter(grad, "vx", scatter_dimension=0, tiled=True)
    grad = halve(grad[0], "vz", 0)
    return grad, dens


def butterfly_sum(x, axes):
    count = lax.axis_size(axes)
    bit = 1
    while bit < count:
        perm = [(i, i ^ bit) for i in range(count)]
        x = x + lax.ppermute(x, axes, perm)
        bit *= 2
    return x


def body(amps, vvvo, occ_gap, vir_gap, pair_gap, block_sizes, roots, triples):
    tri_count = lax.axis_size(TRI)
    me = lax.axis_index(TRI)
    npair = triples.shape[0]
    nocc = occ_gap.shape[0]
    nrow = tri_count * BMAX
    f32, bf16 = jnp.float32, jnp.bfloat16
    slots = jnp.arange(BMAX, dtype=jnp.int32)
    offsets = (jnp.cumsum(block_sizes) - block_sizes).astype(jnp.int32)

    own = roots == me
    own_size = jnp.sum(jnp.where(own, block_sizes, 0))
    own_off = jnp.sum(jnp.where(own, offsets, 0))
    own_gap = occ_gap[jnp.minimum(own_off + slots, nocc - 1)]
    own_live = slots < own_size

    pair_root = roots[triples]
    pair_gap_occ = occ_gap[jnp.minimum(offsets[triples][..., None] + slots, nocc - 1)]
    pair_live = slots < block_sizes[triples][..., None]
    rows = pair_root[..., None] * BMAX + slots

    everything = whole_of(amps, TRI, 0)
    table = joined_along(from_everyone(vvvo, VIR), 1)

    pick = (rows.reshape(-1)[:, None] == jnp.arange(nrow, dtype=jnp.int32)).astype(bf16)
    picked = jnp.einsum("rb,bad->rad", pick, everything, preferred_element_type=bf16)
    proj = jnp.einsum("rad,kdm->rakm", picked, table, preferred_element_type=f32)
    nv, nk, nm = proj.shape[1], proj.shape[2], proj.shape[3]
    proj = proj.reshape(npair, 2, BMAX, nv, nk, nm)
    left, right = proj[:, 0], proj[:, 1]

    base = vir_gap[:, None, None] + own_gap[None, :, None] + pair_gap[None, None, :]
    den = (
        base[None, None, None]
        + pair_gap_occ[:, 0, :, None, None, None, None]
        + pair_gap_occ[:, 1, None, :, None, None, None]
    )
    live = (
        pair_live[:, 0, :, None, None, None, None]
        & pair_live[:, 1, None, :, None, None, None]
        & own_live[None, None, None, None, :, None]
    )
    weighted = jnp.where(live, left[:, :, None] * right[:, None] / den, 0.0)
    dens_part = jnp.sum(weighted * weighted, axis=(0, 1, 2, 4))
    summed = jnp.sum(weighted, axis=2)

    hi_f32 = lax.reduce_precision(summed, exponent_bits=8, mantissa_bits=7)
    hi = hi_f32.astype(bf16)
    lo = (summed - hi_f32).astype(bf16)
    left_rows = picked.reshape(npair, 2, BMAX, nv, -1)[:, 0]
    grad = jnp.einsum("qiad,qiakm->dkm", left_rows, hi, preferred_element_type=f32)
    grad = grad + jnp.einsum("qiad,qiakm->dkm", left_rows, lo, preferred_element_type=f32)
    grad = grad.reshape(lax.axis_size("vx"), lax.axis_size("vz"), lax.axis_size("vc"), -1, grad.shape[1], grad.shape[2])
    grad, density = reduce_tails(grad, dens_part, (0, 1, 2, 3, 4))
    grad = jnp.transpose(grad, (1, 0, 2))
    density = density / float(tri_count * npair)
    return density, grad


def solution(mesh):
    tri_hi = mesh.shape["tri"] // 4
    vir_hi = mesh.shape["vir"] // 4
    finer = Mesh(mesh.devices.reshape(tri_hi, 4, vir_hi, 2, 2), TRI + VIR)
    return jax.shard_map(
        body,
        mesh=finer,
        in_specs=(
            P(TRI, VIR, None),
            P(TRI, VIR, None),
            P(),
            P(VIR),
            P(),
            P(),
            P(),
            P(TRI, None),
        ),
        out_specs=(P(VIR, None), P(TRI, VIR, None)),
        check_vma=False,
    )
```

```python
import jax
import jax.numpy as jnp
from jax import lax
from jax.sharding import Mesh
from jax.sharding import PartitionSpec as P

BMAX = 3
TRI = ("tri_0", "tri_1")
VIR = ("vx", "vz", "vc")


def whole_of(x, axes, dim):
    if not axes:
        return x
    nearer = lax.all_gather(x, axes[-1], axis=dim, tiled=True)
    return whole_of(nearer, axes[:-1], dim)


def from_everyone(x, axis):
    copies = jnp.broadcast_to(x, (lax.axis_size(axis), *x.shape))
    return lax.all_to_all(copies, axis, split_axis=0, concat_axis=0, tiled=True)


def joined_along(pieces, dim):
    pieces = jnp.moveaxis(pieces, 0, dim)
    lengths = pieces.shape
    return pieces.reshape(*lengths[:dim], lengths[dim] * lengths[dim + 1], *lengths[dim + 2 :])


def sent_and_summed(x, axis, dim):
    before, after = (x.shape[:dim], x.shape[dim + 1 :])
    pieces = jnp.moveaxis(x.reshape(*before, lax.axis_size(axis), -1, *after), dim, 0)
    arrived = lax.all_to_all(pieces, axis, split_axis=0, concat_axis=0, tiled=True)
    return arrived.sum(axis=0)


def halve(x, axis, dim):
    mine = lax.axis_index(axis)
    keep = lax.dynamic_index_in_dim(x, mine, axis=dim, keepdims=False)
    send = lax.dynamic_index_in_dim(x, 1 - mine, axis=dim, keepdims=False)
    return keep + lax.ppermute(send, axis, [(0, 1), (1, 0)])


def reduce_tails(grad, dens, tri_bits):
    tri_count = lax.axis_size(TRI)
    grad = halve(grad, "vc", 2)
    for r, bit in enumerate(tri_bits):
        perm = [(i, i ^ (1 << bit)) for i in range(tri_count)]
        dens = dens + lax.ppermute(dens, TRI, perm)
        if r == 0:
            grad = lax.psum_scatter(grad.reshape(-1, *grad.shape[2:]), ("vx", "vz"), scatter_dimension=0, tiled=True)
    return grad[0], dens


def butterfly_sum(x, axes):
    count = lax.axis_size(axes)
    bit = 1
    while bit < count:
        perm = [(i, i ^ bit) for i in range(count)]
        x = x + lax.ppermute(x, axes, perm)
        bit *= 2
    return x


def body(amps, vvvo, occ_gap, vir_gap, pair_gap, block_sizes, roots, triples):
    tri_count = lax.axis_size(TRI)
    me = lax.axis_index(TRI)
    npair = triples.shape[0]
    nocc = occ_gap.shape[0]
    nrow = tri_count * BMAX
    f32, bf16 = jnp.float32, jnp.bfloat16
    slots = jnp.arange(BMAX, dtype=jnp.int32)
    offsets = (jnp.cumsum(block_sizes) - block_sizes).astype(jnp.int32)

    own = roots == me
    own_size = jnp.sum(jnp.where(own, block_sizes, 0))
    own_off = jnp.sum(jnp.where(own, offsets, 0))
    own_gap = occ_gap[jnp.minimum(own_off + slots, nocc - 1)]
    own_live = slots < own_size

    pair_root = roots[triples]
    pair_gap_occ = occ_gap[jnp.minimum(offsets[triples][..., None] + slots, nocc - 1)]
    pair_live = slots < block_sizes[triples][..., None]
    rows = pair_root[..., None] * BMAX + slots

    everything = whole_of(amps, TRI, 0)
    table = joined_along(from_everyone(vvvo, VIR), 1)

    pick = (rows.reshape(-1)[:, None] == jnp.arange(nrow, dtype=jnp.int32)).astype(bf16)
    picked = jnp.einsum("rb,bad->rad", pick, everything, preferred_element_type=bf16)
    proj = jnp.einsum("rad,kdm->rakm", picked, table, preferred_element_type=f32)
    nv, nk, nm = proj.shape[1], proj.shape[2], proj.shape[3]
    proj = proj.reshape(npair, 2, BMAX, nv, nk, nm)
    left, right = proj[:, 0], proj[:, 1]

    base = vir_gap[:, None, None] + own_gap[None, :, None] + pair_gap[None, None, :]
    den = (
        base[None, None, None]
        + pair_gap_occ[:, 0, :, None, None, None, None]
        + pair_gap_occ[:, 1, None, :, None, None, None]
    )
    live = (
        pair_live[:, 0, :, None, None, None, None]
        & pair_live[:, 1, None, :, None, None, None]
        & own_live[None, None, None, None, :, None]
    )
    weighted = jnp.where(live, left[:, :, None] * right[:, None] / den, 0.0)
    dens_part = jnp.sum(weighted * weighted, axis=(0, 1, 2, 4))
    summed = jnp.sum(weighted, axis=2)

    hi_f32 = lax.reduce_precision(summed, exponent_bits=8, mantissa_bits=7)
    hi = hi_f32.astype(bf16)
    lo = (summed - hi_f32).astype(bf16)
    left_rows = picked.reshape(npair, 2, BMAX, nv, -1)[:, 0]
    grad = jnp.einsum("qiad,qiakm->dkm", left_rows, hi, preferred_element_type=f32)
    grad = grad + jnp.einsum("qiad,qiakm->dkm", left_rows, lo, preferred_element_type=f32)
    grad = grad.reshape(lax.axis_size("vx"), lax.axis_size("vz"), lax.axis_size("vc"), -1, grad.shape[1], grad.shape[2])
    grad, density = reduce_tails(grad, dens_part, (0, 1, 2, 3, 4))
    grad = jnp.transpose(grad, (1, 0, 2))
    density = density / float(tri_count * npair)
    return density, grad


def solution(mesh):
    tri_hi = mesh.shape["tri"] // 4
    vir_hi = mesh.shape["vir"] // 4
    finer = Mesh(mesh.devices.reshape(tri_hi, 4, vir_hi, 2, 2), TRI + VIR)
    return jax.shard_map(
        body,
        mesh=finer,
        in_specs=(
            P(TRI, VIR, None),
            P(TRI, VIR, None),
            P(),
            P(VIR),
            P(),
            P(),
            P(),
            P(TRI, None),
        ),
        out_specs=(P(VIR, None), P(TRI, VIR, None)),
        check_vma=False,
    )
```

```python
import jax
import jax.numpy as jnp
from jax import lax
from jax.experimental import pallas as pl
from jax.experimental.pallas import tpu as pltpu
from jax.sharding import Mesh
from jax.sharding import PartitionSpec as P

BMAX = 3
TRI = ("tri_0", "tri_1")
VIR = ("vx", "vz", "vc")


def whole_of(x, axes, dim):
    if not axes:
        return x
    nearer = lax.all_gather(x, axes[-1], axis=dim, tiled=True)
    return whole_of(nearer, axes[:-1], dim)


def from_everyone(x, axis):
    copies = jnp.broadcast_to(x, (lax.axis_size(axis), *x.shape))
    return lax.all_to_all(copies, axis, split_axis=0, concat_axis=0, tiled=True)


def joined_along(pieces, dim):
    pieces = jnp.moveaxis(pieces, 0, dim)
    lengths = pieces.shape
    return pieces.reshape(*lengths[:dim], lengths[dim] * lengths[dim + 1], *lengths[dim + 2 :])


def sent_and_summed(x, axis, dim):
    before, after = (x.shape[:dim], x.shape[dim + 1 :])
    pieces = jnp.moveaxis(x.reshape(*before, lax.axis_size(axis), -1, *after), dim, 0)
    arrived = lax.all_to_all(pieces, axis, split_axis=0, concat_axis=0, tiled=True)
    return arrived.sum(axis=0)


def pick_blocks(starts, table, width):
    count = starts.shape[0]

    def kernel(starts_ref, src_ref, out_ref, sems):
        def issue(p, c):
            pltpu.make_async_copy(
                src_ref.at[pl.ds(starts_ref[p], width)], out_ref.at[pl.ds(p * width, width)], sems.at[p]
            ).start()
            return c

        lax.fori_loop(0, count, issue, 0)

        def finish(p, c):
            pltpu.make_async_copy(
                src_ref.at[pl.ds(0, width)], out_ref.at[pl.ds(p * width, width)], sems.at[p]
            ).wait()
            return c

        lax.fori_loop(0, count, finish, 0)

    return pl.pallas_call(
        kernel,
        grid_spec=pltpu.PrefetchScalarGridSpec(
            num_scalar_prefetch=1,
            grid=(1,),
            in_specs=[pl.BlockSpec(memory_space=pl.ANY)],
            out_specs=pl.BlockSpec(memory_space=pl.ANY),
            scratch_shapes=[pltpu.SemaphoreType.DMA((count,))],
        ),
        out_shape=jax.ShapeDtypeStruct((count * width,) + table.shape[1:], table.dtype),
    )(starts, table)


def halve(x, axis, dim):
    mine = lax.axis_index(axis)
    keep = lax.dynamic_index_in_dim(x, mine, axis=dim, keepdims=False)
    send = lax.dynamic_index_in_dim(x, 1 - mine, axis=dim, keepdims=False)
    return keep + lax.ppermute(send, axis, [(0, 1), (1, 0)])


def reduce_tails(grad, dens, tri_bits):
    tri_count = lax.axis_size(TRI)
    grad = halve(grad, "vc", 2)
    for r, bit in enumerate(tri_bits):
        perm = [(i, i ^ (1 << bit)) for i in range(tri_count)]
        dens = dens + lax.ppermute(dens, TRI, perm)
        if r == 0:
            grad = lax.psum_scatter(grad, "vx", scatter_dimension=0, tiled=True)
    grad = halve(grad[0], "vz", 0)
    return grad, dens


def butterfly_sum(x, axes):
    count = lax.axis_size(axes)
    bit = 1
    while bit < count:
        perm = [(i, i ^ bit) for i in range(count)]
        x = x + lax.ppermute(x, axes, perm)
        bit *= 2
    return x


def body(amps, vvvo, occ_gap, vir_gap, pair_gap, block_sizes, roots, triples):
    tri_count = lax.axis_size(TRI)
    me = lax.axis_index(TRI)
    npair = triples.shape[0]
    nocc = occ_gap.shape[0]
    nrow = tri_count * BMAX
    f32, bf16 = jnp.float32, jnp.bfloat16
    slots = jnp.arange(BMAX, dtype=jnp.int32)
    offsets = (jnp.cumsum(block_sizes) - block_sizes).astype(jnp.int32)

    own = roots == me
    own_size = jnp.sum(jnp.where(own, block_sizes, 0))
    own_off = jnp.sum(jnp.where(own, offsets, 0))
    own_gap = occ_gap[jnp.minimum(own_off + slots, nocc - 1)]
    own_live = slots < own_size

    pair_root = roots[triples]
    pair_gap_occ = occ_gap[jnp.minimum(offsets[triples][..., None] + slots, nocc - 1)]
    pair_live = slots < block_sizes[triples][..., None]
    rows = pair_root[..., None] * BMAX + slots

    everything = whole_of(amps, TRI, 0)
    table = joined_along(from_everyone(vvvo, VIR), 1)

    picked = pick_blocks((pair_root * BMAX).reshape(-1).astype(jnp.int32), everything, BMAX)
    proj = jnp.einsum("rad,kdm->rakm", picked, table, preferred_element_type=f32)
    nv, nk, nm = proj.shape[1], proj.shape[2], proj.shape[3]
    proj = proj.reshape(npair, 2, BMAX, nv, nk, nm)
    left, right = proj[:, 0], proj[:, 1]

    base = vir_gap[:, None, None] + own_gap[None, :, None] + pair_gap[None, None, :]
    den = (
        base[None, None, None]
        + pair_gap_occ[:, 0, :, None, None, None, None]
        + pair_gap_occ[:, 1, None, :, None, None, None]
    )
    live = (
        pair_live[:, 0, :, None, None, None, None]
        & pair_live[:, 1, None, :, None, None, None]
        & own_live[None, None, None, None, :, None]
    )
    weighted = jnp.where(live, left[:, :, None] * right[:, None] / den, 0.0)
    dens_part = jnp.sum(weighted * weighted, axis=(0, 1, 2, 4))
    summed = jnp.sum(weighted, axis=2)

    hi_f32 = lax.reduce_precision(summed, exponent_bits=8, mantissa_bits=7)
    hi = hi_f32.astype(bf16)
    lo = (summed - hi_f32).astype(bf16)
    left_rows = picked.reshape(npair, 2, BMAX, nv, -1)[:, 0]
    grad = jnp.einsum("qiad,qiakm->dkm", left_rows, hi, preferred_element_type=f32)
    grad = grad + jnp.einsum("qiad,qiakm->dkm", left_rows, lo, preferred_element_type=f32)
    grad = grad.reshape(lax.axis_size("vx"), lax.axis_size("vz"), lax.axis_size("vc"), -1, grad.shape[1], grad.shape[2])
    grad, density = reduce_tails(grad, dens_part, (0, 1, 2, 3, 4))
    grad = jnp.transpose(grad, (1, 0, 2))
    density = density / float(tri_count * npair)
    return density, grad


def solution(mesh):
    tri_hi = mesh.shape["tri"] // 4
    vir_hi = mesh.shape["vir"] // 4
    finer = Mesh(mesh.devices.reshape(tri_hi, 4, vir_hi, 2, 2), TRI + VIR)
    return jax.shard_map(
        body,
        mesh=finer,
        in_specs=(
            P(TRI, VIR, None),
            P(TRI, VIR, None),
            P(),
            P(VIR),
            P(),
            P(),
            P(),
            P(TRI, None),
        ),
        out_specs=(P(VIR, None), P(TRI, VIR, None)),
        check_vma=False,
    )
```

```python
import jax
import jax.numpy as jnp
from jax import lax
from jax.sharding import Mesh
from jax.sharding import PartitionSpec as P

BMAX = 3
TRI = ("tri_0", "tri_1")
VIR = ("vx", "vz", "vc")


def whole_of(x, axes, dim):
    if not axes:
        return x
    nearer = lax.all_gather(x, axes[-1], axis=dim, tiled=True)
    return whole_of(nearer, axes[:-1], dim)


def from_everyone(x, axis):
    copies = jnp.broadcast_to(x, (lax.axis_size(axis), *x.shape))
    return lax.all_to_all(copies, axis, split_axis=0, concat_axis=0, tiled=True)


def joined_along(pieces, dim):
    pieces = jnp.moveaxis(pieces, 0, dim)
    lengths = pieces.shape
    return pieces.reshape(*lengths[:dim], lengths[dim] * lengths[dim + 1], *lengths[dim + 2 :])


def sent_and_summed(x, axis, dim):
    before, after = (x.shape[:dim], x.shape[dim + 1 :])
    pieces = jnp.moveaxis(x.reshape(*before, lax.axis_size(axis), -1, *after), dim, 0)
    arrived = lax.all_to_all(pieces, axis, split_axis=0, concat_axis=0, tiled=True)
    return arrived.sum(axis=0)


def halve(x, axis, dim):
    mine = lax.axis_index(axis)
    keep = lax.dynamic_index_in_dim(x, mine, axis=dim, keepdims=False)
    send = lax.dynamic_index_in_dim(x, 1 - mine, axis=dim, keepdims=False)
    return keep + lax.ppermute(send, axis, [(0, 1), (1, 0)])


def reduce_tails(grad, dens, tri_bits):
    tri_count = lax.axis_size(TRI)
    grad = jnp.moveaxis(grad, 1, 2)
    grad = grad.reshape(-1, *grad.shape[2:])
    grad = lax.psum_scatter(grad, ("vx", "vc"), scatter_dimension=0, tiled=True)
    for bit in tri_bits:
        perm = [(i, i ^ (1 << bit)) for i in range(tri_count)]
        dens = dens + lax.ppermute(dens, TRI, perm)
    grad = halve(grad[0], "vz", 0)
    return grad, dens


def butterfly_sum(x, axes):
    count = lax.axis_size(axes)
    bit = 1
    while bit < count:
        perm = [(i, i ^ bit) for i in range(count)]
        x = x + lax.ppermute(x, axes, perm)
        bit *= 2
    return x


def body(amps, vvvo, occ_gap, vir_gap, pair_gap, block_sizes, roots, triples):
    tri_count = lax.axis_size(TRI)
    me = lax.axis_index(TRI)
    npair = triples.shape[0]
    nocc = occ_gap.shape[0]
    nrow = tri_count * BMAX
    f32, bf16 = jnp.float32, jnp.bfloat16
    slots = jnp.arange(BMAX, dtype=jnp.int32)
    offsets = (jnp.cumsum(block_sizes) - block_sizes).astype(jnp.int32)

    own = roots == me
    own_size = jnp.sum(jnp.where(own, block_sizes, 0))
    own_off = jnp.sum(jnp.where(own, offsets, 0))
    own_gap = occ_gap[jnp.minimum(own_off + slots, nocc - 1)]
    own_live = slots < own_size

    pair_root = roots[triples]
    pair_gap_occ = occ_gap[jnp.minimum(offsets[triples][..., None] + slots, nocc - 1)]
    pair_live = slots < block_sizes[triples][..., None]
    rows = pair_root[..., None] * BMAX + slots

    everything = whole_of(amps, TRI, 0)
    table = joined_along(from_everyone(vvvo, VIR), 1)

    pick = (rows.reshape(-1)[:, None] == jnp.arange(nrow, dtype=jnp.int32)).astype(bf16)
    picked = jnp.einsum("rb,bad->rad", pick, everything, preferred_element_type=bf16)
    proj = jnp.einsum("rad,kdm->rakm", picked, table, preferred_element_type=f32)
    nv, nk, nm = proj.shape[1], proj.shape[2], proj.shape[3]
    proj = proj.reshape(npair, 2, BMAX, nv, nk, nm)
    left, right = proj[:, 0], proj[:, 1]

    base = vir_gap[:, None, None] + own_gap[None, :, None] + pair_gap[None, None, :]
    den = (
        base[None, None, None]
        + pair_gap_occ[:, 0, :, None, None, None, None]
        + pair_gap_occ[:, 1, None, :, None, None, None]
    )
    live = (
        pair_live[:, 0, :, None, None, None, None]
        & pair_live[:, 1, None, :, None, None, None]
        & own_live[None, None, None, None, :, None]
    )
    weighted = jnp.where(live, left[:, :, None] * right[:, None] / den, 0.0)
    dens_part = jnp.sum(weighted * weighted, axis=(0, 1, 2, 4))
    summed = jnp.sum(weighted, axis=2)

    hi_f32 = lax.reduce_precision(summed, exponent_bits=8, mantissa_bits=7)
    hi = hi_f32.astype(bf16)
    lo = (summed - hi_f32).astype(bf16)
    left_rows = picked.reshape(npair, 2, BMAX, nv, -1)[:, 0]
    grad = jnp.einsum("qiad,qiakm->dkm", left_rows, hi, preferred_element_type=f32)
    grad = grad + jnp.einsum("qiad,qiakm->dkm", left_rows, lo, preferred_element_type=f32)
    grad = grad.reshape(lax.axis_size("vx"), lax.axis_size("vz"), lax.axis_size("vc"), -1, grad.shape[1], grad.shape[2])
    grad, density = reduce_tails(grad, dens_part, (0, 1, 2, 3, 4))
    grad = jnp.transpose(grad, (1, 0, 2))
    density = density / float(tri_count * npair)
    return density, grad


def solution(mesh):
    tri_hi = mesh.shape["tri"] // 4
    vir_hi = mesh.shape["vir"] // 4
    finer = Mesh(mesh.devices.reshape(tri_hi, 4, vir_hi, 2, 2), TRI + VIR)
    return jax.shard_map(
        body,
        mesh=finer,
        in_specs=(
            P(TRI, VIR, None),
            P(TRI, VIR, None),
            P(),
            P(VIR),
            P(),
            P(),
            P(),
            P(TRI, None),
        ),
        out_specs=(P(VIR, None), P(TRI, VIR, None)),
        check_vma=False,
    )
```

```python
import jax
import jax.numpy as jnp
from jax import lax
from jax.sharding import Mesh
from jax.sharding import PartitionSpec as P

BMAX = 3
TRI = ("tri_0", "tri_1")
VIR = ("vx", "vz", "vc")


def whole_of(x, axes, dim):
    if not axes:
        return x
    nearer = lax.all_gather(x, axes[-1], axis=dim, tiled=True)
    return whole_of(nearer, axes[:-1], dim)


def from_everyone(x, axis):
    copies = jnp.broadcast_to(x, (lax.axis_size(axis), *x.shape))
    return lax.all_to_all(copies, axis, split_axis=0, concat_axis=0, tiled=True)


def joined_along(pieces, dim):
    pieces = jnp.moveaxis(pieces, 0, dim)
    lengths = pieces.shape
    return pieces.reshape(*lengths[:dim], lengths[dim] * lengths[dim + 1], *lengths[dim + 2 :])


def sent_and_summed(x, axis, dim):
    before, after = (x.shape[:dim], x.shape[dim + 1 :])
    pieces = jnp.moveaxis(x.reshape(*before, lax.axis_size(axis), -1, *after), dim, 0)
    arrived = lax.all_to_all(pieces, axis, split_axis=0, concat_axis=0, tiled=True)
    return arrived.sum(axis=0)


def halve(x, axis, dim):
    mine = lax.axis_index(axis)
    keep = lax.dynamic_index_in_dim(x, mine, axis=dim, keepdims=False)
    send = lax.dynamic_index_in_dim(x, 1 - mine, axis=dim, keepdims=False)
    return keep + lax.ppermute(send, axis, [(0, 1), (1, 0)])


def reduce_tails(grad, dens, tri_bits):
    tri_count = lax.axis_size(TRI)
    grad = halve(grad, "vc", 2)
    for r, bit in enumerate(tri_bits):
        perm = [(i, i ^ (1 << bit)) for i in range(tri_count)]
        dens = dens + lax.ppermute(dens, TRI, perm)
        if r == 0:
            grad = lax.psum_scatter(grad, "vx", scatter_dimension=0, tiled=True)
    grad = halve(grad[0], "vz", 0)
    return grad, dens


def butterfly_sum(x, axes):
    count = lax.axis_size(axes)
    bit = 1
    while bit < count:
        perm = [(i, i ^ bit) for i in range(count)]
        x = x + lax.ppermute(x, axes, perm)
        bit *= 2
    return x


def body(amps, vvvo, occ_gap, vir_gap, pair_gap, block_sizes, roots, triples):
    tri_count = lax.axis_size(TRI)
    me = lax.axis_index(TRI)
    npair = triples.shape[0]
    nocc = occ_gap.shape[0]
    nrow = tri_count * BMAX
    f32, bf16 = jnp.float32, jnp.bfloat16
    slots = jnp.arange(BMAX, dtype=jnp.int32)
    offsets = (jnp.cumsum(block_sizes) - block_sizes).astype(jnp.int32)

    own = roots == me
    own_size = jnp.sum(jnp.where(own, block_sizes, 0))
    own_off = jnp.sum(jnp.where(own, offsets, 0))
    own_gap = occ_gap[jnp.minimum(own_off + slots, nocc - 1)]
    own_live = slots < own_size

    pair_root = roots[triples]
    pair_gap_occ = occ_gap[jnp.minimum(offsets[triples][..., None] + slots, nocc - 1)]
    pair_live = slots < block_sizes[triples][..., None]
    rows = pair_root[..., None] * BMAX + slots

    everything = lax.all_gather(joined_along(from_everyone(amps, "tri_1"), 0), "tri_0", axis=0, tiled=True)
    table = joined_along(from_everyone(vvvo, VIR), 1)

    pick = (rows.reshape(-1)[:, None] == jnp.arange(nrow, dtype=jnp.int32)).astype(bf16)
    picked = jnp.einsum("rb,bad->rad", pick, everything, preferred_element_type=bf16)
    proj = jnp.einsum("rad,kdm->rakm", picked, table, preferred_element_type=f32)
    nv, nk, nm = proj.shape[1], proj.shape[2], proj.shape[3]
    proj = proj.reshape(npair, 2, BMAX, nv, nk, nm)
    left, right = proj[:, 0], proj[:, 1]

    base = vir_gap[:, None, None] + own_gap[None, :, None] + pair_gap[None, None, :]
    den = (
        base[None, None, None]
        + pair_gap_occ[:, 0, :, None, None, None, None]
        + pair_gap_occ[:, 1, None, :, None, None, None]
    )
    live = (
        pair_live[:, 0, :, None, None, None, None]
        & pair_live[:, 1, None, :, None, None, None]
        & own_live[None, None, None, None, :, None]
    )
    weighted = jnp.where(live, left[:, :, None] * right[:, None] / den, 0.0)
    dens_part = jnp.sum(weighted * weighted, axis=(0, 1, 2, 4))
    summed = jnp.sum(weighted, axis=2)

    hi_f32 = lax.reduce_precision(summed, exponent_bits=8, mantissa_bits=7)
    hi = hi_f32.astype(bf16)
    lo = (summed - hi_f32).astype(bf16)
    left_rows = picked.reshape(npair, 2, BMAX, nv, -1)[:, 0]
    grad = jnp.einsum("qiad,qiakm->dkm", left_rows, hi, preferred_element_type=f32)
    grad = grad + jnp.einsum("qiad,qiakm->dkm", left_rows, lo, preferred_element_type=f32)
    grad = grad.reshape(lax.axis_size("vx"), lax.axis_size("vz"), lax.axis_size("vc"), -1, grad.shape[1], grad.shape[2])
    grad, density = reduce_tails(grad, dens_part, (0, 1, 2, 3, 4))
    grad = jnp.transpose(grad, (1, 0, 2))
    density = density / float(tri_count * npair)
    return density, grad


def solution(mesh):
    tri_hi = mesh.shape["tri"] // 4
    vir_hi = mesh.shape["vir"] // 4
    finer = Mesh(mesh.devices.reshape(tri_hi, 4, vir_hi, 2, 2), TRI + VIR)
    return jax.shard_map(
        body,
        mesh=finer,
        in_specs=(
            P(TRI, VIR, None),
            P(TRI, VIR, None),
            P(),
            P(VIR),
            P(),
            P(),
            P(),
            P(TRI, None),
        ),
        out_specs=(P(VIR, None), P(TRI, VIR, None)),
        check_vma=False,
    )
```

```python
import jax
import jax.numpy as jnp
from jax import lax
from jax.sharding import Mesh
from jax.sharding import PartitionSpec as P

BMAX = 3
TRI = ("tri_0", "tri_1")
VIR = ("vx", "vz", "vc")


def whole_of(x, axes, dim):
    if not axes:
        return x
    nearer = lax.all_gather(x, axes[-1], axis=dim, tiled=True)
    return whole_of(nearer, axes[:-1], dim)


def from_everyone(x, axis):
    copies = jnp.broadcast_to(x, (lax.axis_size(axis), *x.shape))
    return lax.all_to_all(copies, axis, split_axis=0, concat_axis=0, tiled=True)


def joined_along(pieces, dim):
    pieces = jnp.moveaxis(pieces, 0, dim)
    lengths = pieces.shape
    return pieces.reshape(*lengths[:dim], lengths[dim] * lengths[dim + 1], *lengths[dim + 2 :])


def sent_and_summed(x, axis, dim):
    before, after = (x.shape[:dim], x.shape[dim + 1 :])
    pieces = jnp.moveaxis(x.reshape(*before, lax.axis_size(axis), -1, *after), dim, 0)
    arrived = lax.all_to_all(pieces, axis, split_axis=0, concat_axis=0, tiled=True)
    return arrived.sum(axis=0)


def halve(x, axis, dim):
    mine = lax.axis_index(axis)
    keep = lax.dynamic_index_in_dim(x, mine, axis=dim, keepdims=False)
    send = lax.dynamic_index_in_dim(x, 1 - mine, axis=dim, keepdims=False)
    return keep + lax.ppermute(send, axis, [(0, 1), (1, 0)])


def reduce_tails(grad, dens, tri_bits):
    tri_count = lax.axis_size(TRI)
    grad = halve(grad, "vc", 2)
    for r, bit in enumerate(tri_bits):
        perm = [(i, i ^ (1 << bit)) for i in range(tri_count)]
        dens = dens + lax.ppermute(dens, TRI, perm)
        if r == 0:
            grad = lax.psum_scatter(grad, "vx", scatter_dimension=0, tiled=True)
    grad = halve(grad[0], "vz", 0)
    return grad, dens


def butterfly_sum(x, axes):
    count = lax.axis_size(axes)
    bit = 1
    while bit < count:
        perm = [(i, i ^ bit) for i in range(count)]
        x = x + lax.ppermute(x, axes, perm)
        bit *= 2
    return x


def body(amps, vvvo, occ_gap, vir_gap, pair_gap, block_sizes, roots, triples):
    tri_count = lax.axis_size(TRI)
    me = lax.axis_index(TRI)
    npair = triples.shape[0]
    nocc = occ_gap.shape[0]
    nrow = tri_count * BMAX
    f32, bf16 = jnp.float32, jnp.bfloat16
    slots = jnp.arange(BMAX, dtype=jnp.int32)
    offsets = (jnp.cumsum(block_sizes) - block_sizes).astype(jnp.int32)

    own = roots == me
    own_size = jnp.sum(jnp.where(own, block_sizes, 0))
    own_off = jnp.sum(jnp.where(own, offsets, 0))
    own_gap = occ_gap[jnp.minimum(own_off + slots, nocc - 1)]
    own_live = slots < own_size

    pair_root = roots[triples]
    pair_gap_occ = occ_gap[jnp.minimum(offsets[triples][..., None] + slots, nocc - 1)]
    pair_live = slots < block_sizes[triples][..., None]
    rows = pair_root[..., None] * BMAX + slots

    everything = whole_of(amps, TRI, 0)
    table = joined_along(from_everyone(vvvo, VIR), 1)

    pick = (rows.reshape(-1)[:, None] == jnp.arange(nrow, dtype=jnp.int32)).astype(bf16)
    flat = everything.reshape(everything.shape[0], -1)
    picked = jnp.dot(pick, flat, preferred_element_type=bf16).reshape(-1, *everything.shape[1:])
    proj = jnp.einsum("rad,kdm->rakm", picked, table, preferred_element_type=f32)
    nv, nk, nm = proj.shape[1], proj.shape[2], proj.shape[3]
    proj = proj.reshape(npair, 2, BMAX, nv, nk, nm)
    left, right = proj[:, 0], proj[:, 1]

    base = vir_gap[:, None, None] + own_gap[None, :, None] + pair_gap[None, None, :]
    den = (
        base[None, None, None]
        + pair_gap_occ[:, 0, :, None, None, None, None]
        + pair_gap_occ[:, 1, None, :, None, None, None]
    )
    live = (
        pair_live[:, 0, :, None, None, None, None]
        & pair_live[:, 1, None, :, None, None, None]
        & own_live[None, None, None, None, :, None]
    )
    weighted = jnp.where(live, left[:, :, None] * right[:, None] / den, 0.0)
    dens_part = jnp.sum(weighted * weighted, axis=(0, 1, 2, 4))
    summed = jnp.sum(weighted, axis=2)

    hi_f32 = lax.reduce_precision(summed, exponent_bits=8, mantissa_bits=7)
    hi = hi_f32.astype(bf16)
    lo = (summed - hi_f32).astype(bf16)
    left_rows = picked.reshape(npair, 2, BMAX, nv, -1)[:, 0]
    grad = jnp.einsum("qiad,qiakm->dkm", left_rows, hi, preferred_element_type=f32)
    grad = grad + jnp.einsum("qiad,qiakm->dkm", left_rows, lo, preferred_element_type=f32)
    grad = grad.reshape(lax.axis_size("vx"), lax.axis_size("vz"), lax.axis_size("vc"), -1, grad.shape[1], grad.shape[2])
    grad, density = reduce_tails(grad, dens_part, (0, 1, 2, 3, 4))
    grad = jnp.transpose(grad, (1, 0, 2))
    density = density / float(tri_count * npair)
    return density, grad


def solution(mesh):
    tri_hi = mesh.shape["tri"] // 4
    vir_hi = mesh.shape["vir"] // 4
    finer = Mesh(mesh.devices.reshape(tri_hi, 4, vir_hi, 2, 2), TRI + VIR)
    return jax.shard_map(
        body,
        mesh=finer,
        in_specs=(
            P(TRI, VIR, None),
            P(TRI, VIR, None),
            P(),
            P(VIR),
            P(),
            P(),
            P(),
            P(TRI, None),
        ),
        out_specs=(P(VIR, None), P(TRI, VIR, None)),
        check_vma=False,
    )
```

```python
import jax
import jax.numpy as jnp
from jax import lax
from jax.sharding import Mesh
from jax.sharding import PartitionSpec as P


BMAX = 3
TRI = ("tri_0", "tri_1")
VIR = ("vx", "vz", "vc")


def whole_of(x, axes, dim):
    if not axes:
        return x
    nearer = lax.all_gather(x, axes[-1], axis=dim, tiled=True)
    return whole_of(nearer, axes[:-1], dim)


def from_everyone(x, axis):
    copies = jnp.broadcast_to(x, (lax.axis_size(axis), *x.shape))
    return lax.all_to_all(copies, axis, split_axis=0, concat_axis=0, tiled=True)


def joined_along(pieces, dim):
    pieces = jnp.moveaxis(pieces, 0, dim)
    lengths = pieces.shape
    return pieces.reshape(*lengths[:dim], lengths[dim] * lengths[dim + 1], *lengths[dim + 2 :])


def halve(x, axis, dim):
    mine = lax.axis_index(axis)
    keep = lax.dynamic_index_in_dim(x, mine, axis=dim, keepdims=False)
    send = lax.dynamic_index_in_dim(x, 1 - mine, axis=dim, keepdims=False)
    return keep + lax.ppermute(send, axis, [(0, 1), (1, 0)])


def reduce_tails(grad, dens, tri_bits):
    tri_count = lax.axis_size(TRI)
    grad = halve(grad, "vc", 2)
    for r, bit in enumerate(tri_bits):
        perm = [(i, i ^ (1 << bit)) for i in range(tri_count)]
        dens = dens + lax.ppermute(dens, TRI, perm)
        if r == 0:
            grad = lax.psum_scatter(grad, "vx", scatter_dimension=0, tiled=True)
    grad = halve(grad[0], "vz", 0)
    return grad, dens


def body_inner(amps, vvvo, occ_gap, vir_gap, pair_gap, block_sizes, roots, triples):
    tri_count = lax.axis_size(TRI)
    me = lax.axis_index(TRI)
    npair = triples.shape[0]
    nocc = occ_gap.shape[0]
    nrow = tri_count * BMAX
    f32, bf16 = jnp.float32, jnp.bfloat16
    slots = jnp.arange(BMAX, dtype=jnp.int32)
    offsets = (jnp.cumsum(block_sizes) - block_sizes).astype(jnp.int32)

    own = roots == me
    own_size = jnp.sum(jnp.where(own, block_sizes, 0))
    own_off = jnp.sum(jnp.where(own, offsets, 0))
    own_gap = occ_gap[jnp.minimum(own_off + slots, nocc - 1)]
    own_live = slots < own_size

    pair_root = roots[triples]
    pair_gap_occ = occ_gap[jnp.minimum(offsets[triples][..., None] + slots, nocc - 1)]
    pair_live = slots < block_sizes[triples][..., None]
    rows = pair_root[..., None] * BMAX + slots

    everything = whole_of(amps, TRI, 0)
    table = joined_along(from_everyone(vvvo, VIR), 1)

    pick = (rows.reshape(-1)[:, None] == jnp.arange(nrow, dtype=jnp.int32)).astype(bf16)
    picked = jnp.einsum("rb,bad->rad", pick, everything, preferred_element_type=bf16)
    proj = jnp.einsum("rad,kdm->rakm", picked, table, preferred_element_type=f32)
    nv, nk, nm = proj.shape[1], proj.shape[2], proj.shape[3]
    proj = proj.reshape(npair, 2, BMAX, nv, nk, nm)
    left, right = proj[:, 0], proj[:, 1]

    base = vir_gap[:, None, None] + own_gap[None, :, None] + pair_gap[None, None, :]
    den = (
        base[None, None, None]
        + pair_gap_occ[:, 0, :, None, None, None, None]
        + pair_gap_occ[:, 1, None, :, None, None, None]
    )
    live = (
        pair_live[:, 0, :, None, None, None, None]
        & pair_live[:, 1, None, :, None, None, None]
        & own_live[None, None, None, None, :, None]
    )
    weighted = jnp.where(live, left[:, :, None] * right[:, None] / den, 0.0)
    dens_part = jnp.sum(weighted * weighted, axis=(0, 1, 2, 4))
    summed = jnp.sum(weighted, axis=2)

    hi_f32 = lax.reduce_precision(summed, exponent_bits=8, mantissa_bits=7)
    hi = hi_f32.astype(bf16)
    lo = (summed - hi_f32).astype(bf16)
    left_rows = picked.reshape(npair, 2, BMAX, nv, -1)[:, 0]
    grad = jnp.einsum("qiad,qiakm->dkm", left_rows, hi, preferred_element_type=f32)
    grad = grad + jnp.einsum("qiad,qiakm->dkm", left_rows, lo, preferred_element_type=f32)
    grad = grad.reshape(lax.axis_size("vx"), lax.axis_size("vz"), lax.axis_size("vc"), -1, grad.shape[1], grad.shape[2])
    grad, density = reduce_tails(grad, dens_part, (4, 0, 1, 2, 3))
    grad = jnp.transpose(grad, (1, 0, 2))
    density = density / float(tri_count * npair)
    return density, grad


def solution(mesh):
    tri_hi = mesh.shape["tri"] // 4
    vir_hi = mesh.shape["vir"] // 4
    finer = Mesh(mesh.devices.reshape(tri_hi, 4, vir_hi, 2, 2), TRI + VIR)
    return jax.shard_map(
        body_inner,
        mesh=finer,
        in_specs=(
            P(TRI, VIR, None),
            P(TRI, VIR, None),
            P(),
            P(VIR),
            P(),
            P(),
            P(),
            P(TRI, None),
        ),
        out_specs=(P(VIR, None), P(TRI, VIR, None)),
        check_vma=False,
    )
```
